256 devices in a mesh: seg: 8 (over y, core), sec: 32 (over x, z).
Axes of the slice: x: 4, y: 4, z: 8, core: 2. Of those that a mesh axis runs over, the one named last changes fastest.
Arguments:
- theta_in: float32 [8, 64, 128, 128], P('seg', 'sec'), may hold values from -6 to 6
- left_env: float32 [9, 64, 128, 128], P(None, 'sec'), may hold values from -0.0017089844 to 0.0017089844
- site_maps: float32 [8, 64, 128, 128], P('seg', 'sec'), may hold values from -1 to 2, as said below
- right_env: float32 [8, 9, 64, 128, 128], P('seg', None, 'sec'), may hold values from -8 to 8
- mpo_mask: int32 [9, 64], P(None, 'sec'), may hold values 0 or 1
- ranks: int32 [8, 64], P('seg', 'sec'), may hold values from 64 to 128
Outputs:
- theta_out: float32 [8, 64, 128, 128], P('seg', 'sec')
- density: float32 [8, 64, 128, 128], P('seg', 'sec')
The draws below stay inside these ranges and needn't reach their ends.
Inputs may be any that keep to these rules, and one draw needn't show every extreme that they name: `site_maps`: each block of a segment's map is the identity plus a full matrix of entries of size about 1 / (4 sqrt(128)).
All inputs are finite; a program needn't handle non-finite values. No bound on the sum of `mpo_mask` on one device may be relied on, other than what follows from the above.
Results may differ from the reference program's by a relative error of at most 0.0003.
Values sent between devices are 32-bit elements; how exact they have to be, the bound alone decides.
No kernel may reach another device: no remote copies, remote signals or barrier semaphores. Data moves between devices by JAX's collectives and lax.ppermute only.
A program may use at most 64 MiB of HBM per device.

```python
import math
import jax
import jax.numpy as jnp
from jax import lax

SB = 128
W = 9
ITERS = 4
NSEG = 8
NSEC = 64


def draw_site_maps(key, part):
    noise = jax.random.normal(key, (NSEG, NSEC, SB, SB), jnp.float32)
    return jnp.eye(SB, dtype=jnp.float32) + 0.25 * noise / math.sqrt(SB)


def draw_right_env(key, part):
    first = jax.random.fold_in(key, 0)
    noise = jax.random.normal(first, (NSEG, W, NSEC, SB, SB), jnp.float32)
    noise = jnp.clip(noise, -5.0, 5.0)
    position = jnp.arange(NSEC, dtype=jnp.float32) / max(NSEC - 1, 1)
    scale = jnp.exp(math.log(3.0) * position)
    return noise * scale[None, None, :, None, None] / math.sqrt(SB)


def with_ends(entries, rng, least, largest):
    dims = entries.shape
    place = [jax.random.randint(jax.random.fold_in(rng, axis), (), 0, dims[axis]) for axis in range(len(dims))]
    entries = entries.at[tuple(place)].set(least)
    longest = dims.index(max(dims))
    place[longest] = (place[longest] + 1) % dims[longest]
    return entries.at[tuple(place)].set(largest)


def shard_levels(rng, dims, cuts, smallest, largest):
    gain, own = 1.0, jax.random.fold_in(rng, 6)
    for dim, blocks in cuts:
        heights = jnp.exp(jax.random.uniform(jax.random.fold_in(own, dim), (blocks,), jnp.float32, smallest / len(cuts), largest / len(cuts)))
        gain = gain * jnp.repeat(heights, dims[dim] // blocks).reshape([-1 if axis == dim else 1 for axis in range(len(dims))])
    return gain


def bell_draw(key, dims, spread, limit, cuts=(), held_as=jnp.bfloat16):
    array = jax.random.normal(key, dims, jnp.float32) * spread
    if len(cuts) > 0:
        array = shard_levels(key, dims, cuts, -0.22, 0.18) * array
    return jnp.clip(array, min=-limit, max=limit).astype(held_as)


def setup_inputs(seed: int = 0) -> dict:
    splits = jax.random.split(jax.random.key(seed), 7)
    return {
        "theta_in": bell_draw(splits[0], (NSEG, NSEC, SB, SB), 1.0, 6.0, ((0, 8), (1, 32)), jnp.float32),
        "left_env": bell_draw(splits[1], (W, NSEC, SB, SB), (90000 * SB) ** -0.5, 0.0017089844, ((1, 32),), jnp.float32),
        "site_maps": draw_site_maps(jax.random.fold_in(splits[6], 71), 0),
        "right_env": draw_right_env(jax.random.fold_in(splits[6], 71), 0),
        "mpo_mask": with_ends((jax.random.randint(splits[4], (W, NSEC), 0, 4) < 3).astype(jnp.int32), jax.random.fold_in(splits[4], 1), 0, 1),
        "ranks": with_ends(jax.random.randint(splits[5], (NSEG, NSEC), SB // 2, SB + 1), jax.random.fold_in(splits[5], 1), SB // 2, SB).astype(jnp.int32),
    }


HIGH = lax.Precision.HIGHEST
EPS = 1e-06

def advance_env(env, maps):
    partial_env = jnp.einsum('wkac,kcd->wkad', env, maps, precision=HIGH)
    return jnp.einsum('kab,wkad->wkbd', maps, partial_env, precision=HIGH)

def shifted_terms(padded, count, blocks):
    pieces = []
    for term in range(count):
        offset = 1 + term % 3 - 1
        pieces.append(padded[term, offset:offset + blocks])
    return jnp.stack(pieces, axis=0)

def reference(theta_in, left_env, site_maps, right_env, mpo_mask, ranks):
    keep_terms = mpo_mask.astype(jnp.float32)[:, :, None, None]
    env = left_env
    vectors = []
    densities = []
    for segment in range(NSEG):
        if segment > 0:
            env = advance_env(env, site_maps[segment - 1])
        vector = theta_in[segment]
        right = right_env[segment]
        weighted = env * keep_terms
        for step in range(ITERS):
            products = jnp.einsum('kab,wkbc->wkac', vector, right, precision=HIGH)
            padded = jnp.pad(products, ((0, 0), (1, 1), (0, 0), (0, 0)))
            gathered = shifted_terms(padded, W, NSEC)
            image = jnp.einsum('wkab,wkbc->kac', weighted, gathered, precision=HIGH)
            total = jnp.sum(image * image)
            vector = image * lax.rsqrt(total / (NSEC * SB * SB) + EPS)
        rows = lax.broadcasted_iota(jnp.int32, (NSEC, SB), 1) < ranks[segment][:, None]
        trimmed = vector * rows.astype(jnp.float32)[:, :, None]
        density = jnp.einsum('kab,kcb->kac', trimmed, trimmed, precision=HIGH) / SB
        vectors.append(vector)
        densities.append(density)
    return (jnp.stack(vectors, axis=0), jnp.stack(densities, axis=0))
```

```python
import jax
import jax.numpy as jnp
from jax import lax
from jax.sharding import PartitionSpec as P

ITERS = 4


HIGH = lax.Precision.HIGHEST
EPS = 1e-06
LIFT = 1024.0


def shifted(block, axis, step):
    count = lax.axis_size(axis)
    route = [(i, i + step) for i in range(count) if 0 <= i + step < count]
    return lax.ppermute(block, axis, route)


def gathered_sum(value, axis):
    count = lax.axis_size(axis)
    spread = jnp.broadcast_to(value.reshape(1, 1), (count, 1))
    return jnp.sum(lax.all_to_all(spread, axis, 0, 0, tiled=True))


def mm(spec, a, b):
    return jnp.einsum(spec, a, b, precision=HIGH)


def left_environment(left_env, maps):
    segments = lax.axis_size("seg")
    segment = lax.axis_index("seg")
    spread = jnp.broadcast_to(maps[None], (segments,) + maps.shape)
    every = lax.all_to_all(spread, "seg", 0, 0, tiled=True)
    width = maps.shape[-1]
    prefix = jnp.broadcast_to(jnp.eye(width, dtype=jnp.float32), maps.shape)
    for step in range(segments - 1):
        grown = mm("kab,kbc->kac", prefix, every[step])
        prefix = jnp.where(step < segment, grown, prefix)
    right_side = mm("wkbc,kcd->wkbd", left_env, prefix)
    return mm("kba,wkbd->wkad", prefix, right_side)


def apply_terms(vector, right, ordered):
    products = mm("kab,wkbc->wkac", vector, right)
    from_left = shifted(products[0::3, 1], "sec", 1)
    from_right = shifted(products[2::3, 0], "sec", -1)
    lower = jnp.stack([from_left, products[0::3, 0]], axis=1)
    upper = jnp.stack([products[2::3, 1], from_right], axis=1)
    terms = jnp.concatenate([lower, products[1::3], upper], axis=0)
    return mm("wkab,wkbc->kac", ordered, terms)


def per_device(theta_in, left_env, site_maps, right_env, mpo_mask, ranks):
    vector = theta_in[0]
    maps = site_maps[0]
    right = right_env[0]
    blocks = vector.shape[0]
    width = vector.shape[1]
    cells = lax.axis_size("sec") * blocks * width * width
    env = left_environment(left_env, maps)
    weighted = env * mpo_mask.astype(jnp.float32)[:, :, None, None]
    ordered = jnp.concatenate([weighted[0::3], weighted[1::3], weighted[2::3]], axis=0)
    current = apply_terms(vector, right, ordered)
    for step in range(ITERS):
        total = gathered_sum(jnp.sum(current * current), "sec")
        scale = lax.rsqrt(total / cells + EPS)
        if step + 1 < ITERS:
            image = apply_terms(current * LIFT, right, ordered)
            current = image * (scale / LIFT)
        else:
            current = current * scale
    rows = lax.broadcasted_iota(jnp.int32, (blocks, width), 1) < ranks[0][:, None]
    trimmed = current * rows.astype(jnp.float32)[:, :, None]
    density = mm("kab,kcb->kac", trimmed, trimmed) / width
    return (current[None], density[None])


def solution(mesh):
    return jax.shard_map(
        per_device,
        mesh=mesh,
        in_specs=(
            P("seg", "sec", None, None),
            P(None, "sec", None, None),
            P("seg", "sec", None, None),
            P("seg", None, "sec", None, None),
            P(None, "sec"),
            P("seg", "sec"),
        ),
        out_specs=(P("seg", "sec", None, None), P("seg", "sec", None, None)),
        check_vma=False,
    )
```

```python
import jax
import jax.numpy as jnp
from jax import lax
from jax.sharding import PartitionSpec as P

ITERS = 4


HIGH = lax.Precision.HIGHEST
EPS = 1e-06
LIFT = 1024.0


def shifted(block, axis, step):
    count = lax.axis_size(axis)
    route = [(i, i + step) for i in range(count) if 0 <= i + step < count]
    return lax.ppermute(block, axis, route)


def gathered_sum(vector, axis):
    count = lax.axis_size(axis)
    row = jnp.sum(vector * vector, axis=(0, 1))
    spread = jnp.broadcast_to(row[None], (count, row.shape[0]))
    return jnp.sum(lax.all_to_all(spread, axis, 0, 0, tiled=True))


def mm(spec, a, b):
    return jnp.einsum(spec, a, b, precision=HIGH)


def left_environment(left_env, maps):
    segments = lax.axis_size("seg")
    segment = lax.axis_index("seg")
    spread = jnp.broadcast_to(maps[None], (segments,) + maps.shape)
    every = lax.all_to_all(spread, "seg", 0, 0, tiled=True)
    width = maps.shape[-1]
    prefix = jnp.broadcast_to(jnp.eye(width, dtype=jnp.float32), maps.shape)
    for step in range(segments - 1):
        grown = mm("kab,kbc->kac", prefix, every[step])
        prefix = jnp.where(step < segment, grown, prefix)
    right_side = mm("kwbc,kcd->kwbd", left_env, prefix)
    return mm("kba,kwbd->kwad", prefix, right_side)


def grouped(terms, axis):
    pick = lambda start: lax.slice_in_dim(terms, start, None, 3, axis=axis)
    return jnp.concatenate([pick(0), pick(1), pick(2)], axis=axis)


def apply_terms(vector, right, ordered):
    products = mm("kab,kwbc->kwac", vector, right)
    group = right.shape[1] // 3
    from_left = shifted(products[1, :group], "sec", 1)
    from_right = shifted(products[0, 2 * group :], "sec", -1)
    first = jnp.concatenate([from_left, products[0, group : 2 * group], products[1, 2 * group :]], axis=0)
    second = jnp.concatenate([products[0, :group], products[1, group : 2 * group], from_right], axis=0)
    terms = jnp.stack([first, second], axis=0)
    return lax.optimization_barrier(mm("kwab,kwbc->kac", ordered, terms))


def per_device(theta_in, left_env, site_maps, right_env, mpo_mask, ranks):
    vector = theta_in[0]
    maps = site_maps[0]
    right = grouped(jnp.swapaxes(right_env[0], 0, 1), 1)
    blocks = vector.shape[0]
    width = vector.shape[1]
    cells = lax.axis_size("sec") * blocks * width * width
    env = left_environment(jnp.swapaxes(left_env, 0, 1), maps)
    weighted = env * jnp.swapaxes(mpo_mask, 0, 1).astype(jnp.float32)[:, :, None, None]
    ordered = grouped(weighted, 1)
    current = apply_terms(vector, right, ordered)
    for step in range(ITERS):
        total = gathered_sum(current, "sec")
        scale = lax.rsqrt(total / cells + EPS)
        if step + 1 < ITERS:
            image = apply_terms(current * LIFT, right, ordered)
            current = image * (scale / LIFT)
        else:
            current = current * scale
    rows = lax.broadcasted_iota(jnp.int32, (blocks, width), 1) < ranks[0][:, None]
    trimmed = current * rows.astype(jnp.float32)[:, :, None]
    density = mm("kab,kcb->kac", trimmed, trimmed) / width
    return (current[None], density[None])


def solution(mesh):
    return jax.shard_map(
        per_device,
        mesh=mesh,
        in_specs=(
            P("seg", "sec", None, None),
            P(None, "sec", None, None),
            P("seg", "sec", None, None),
            P("seg", None, "sec", None, None),
            P(None, "sec"),
            P("seg", "sec"),
        ),
        out_specs=(P("seg", "sec", None, None), P("seg", "sec", None, None)),
        check_vma=False,
    )
```

```python
import jax
import jax.numpy as jnp
from jax import lax
from jax.sharding import PartitionSpec as P

ITERS = 4


HIGH = lax.Precision.HIGHEST
EPS = 1e-06
LIFT = 1024.0
SHRINK = 2.0**-50


def shifted(block, axis, step):
    count = lax.axis_size(axis)
    route = [(i, i + step) for i in range(count) if 0 <= i + step < count]
    return lax.ppermute(block, axis, route)


def gathered_sums(values, axis):
    count = lax.axis_size(axis)
    row = jnp.stack(values)
    spread = jnp.broadcast_to(row[None], (count, row.shape[0]))
    return jnp.sum(lax.all_to_all(spread, axis, 0, 0, tiled=True), axis=0)


def mm(spec, a, b):
    return jnp.einsum(spec, a, b, precision=HIGH)


def left_environment(left_env, maps):
    segments = lax.axis_size("seg")
    segment = lax.axis_index("seg")
    spread = jnp.broadcast_to(maps[None], (segments,) + maps.shape)
    every = lax.all_to_all(spread, "seg", 0, 0, tiled=True)
    width = maps.shape[-1]
    prefix = jnp.broadcast_to(jnp.eye(width, dtype=jnp.float32), maps.shape)
    for step in range(segments - 1):
        grown = mm("kab,kbc->kac", prefix, every[step])
        prefix = jnp.where(step < segment, grown, prefix)
    right_side = mm("wkbc,kcd->wkbd", left_env, prefix)
    return mm("kba,wkbd->wkad", prefix, right_side)


def apply_terms(vector, right, ordered):
    products = mm("kab,wkbc->wkac", vector, right)
    from_left = shifted(products[0::3, 1], "sec", 1)
    from_right = shifted(products[2::3, 0], "sec", -1)
    lower = jnp.stack([from_left, products[0::3, 0]], axis=1)
    upper = jnp.stack([products[2::3, 1], from_right], axis=1)
    terms = jnp.concatenate([lower, products[1::3], upper], axis=0)
    return mm("wkab,wkbc->kac", ordered, terms)


def square_sums(normal, lifted):
    return [jnp.sum(normal * normal), jnp.sum(lifted * lifted), jnp.sum(jnp.square(lifted * SHRINK))]


def scales(sums, cells):
    first = lax.rsqrt(sums[0] / cells + EPS)
    step = first / LIFT
    plain = step * step * sums[1]
    shrunk = jnp.square(step / SHRINK) * sums[2]
    second = lax.rsqrt(jnp.where(jnp.isfinite(sums[1]), plain, shrunk) / cells + EPS)
    return first, second


def per_device(theta_in, left_env, site_maps, right_env, mpo_mask, ranks):
    vector = theta_in[0]
    maps = site_maps[0]
    right = right_env[0]
    blocks = vector.shape[0]
    width = vector.shape[1]
    cells = lax.axis_size("sec") * blocks * width * width
    env = left_environment(left_env, maps)
    weighted = env * mpo_mask.astype(jnp.float32)[:, :, None, None]
    ordered = jnp.concatenate([weighted[0::3], weighted[1::3], weighted[2::3]], axis=0)
    current = apply_terms(vector, right, ordered)
    for pair in range(ITERS // 2):
        lifted = apply_terms(current * LIFT, right, ordered)
        first, second = scales(gathered_sums(square_sums(current, lifted), "sec"), cells)
        current = lifted * (first / LIFT)
        if 2 * pair + 2 < ITERS:
            current = apply_terms(current * LIFT, right, ordered) * (second / LIFT)
        else:
            current = current * second
    rows = lax.broadcasted_iota(jnp.int32, (blocks, width), 1) < ranks[0][:, None]
    trimmed = current * rows.astype(jnp.float32)[:, :, None]
    density = mm("kab,kcb->kac", trimmed, trimmed) / width
    return (current[None], density[None])


def solution(mesh):
    return jax.shard_map(
        per_device,
        mesh=mesh,
        in_specs=(
            P("seg", "sec", None, None),
            P(None, "sec", None, None),
            P("seg", "sec", None, None),
            P("seg", None, "sec", None, None),
            P(None, "sec"),
            P("seg", "sec"),
        ),
        out_specs=(P("seg", "sec", None, None), P("seg", "sec", None, None)),
        check_vma=False,
    )
```

```python
import jax
import jax.numpy as jnp
from jax import lax
from jax.sharding import PartitionSpec as P

ITERS = 4


HIGH = lax.Precision.HIGHEST
EPS = 1e-06
LIFT = 1024.0
SHRINK = 2.0**-50


def shifted(block, axis, step):
    count = lax.axis_size(axis)
    route = [(i, i + step) for i in range(count) if 0 <= i + step < count]
    return lax.ppermute(block, axis, route)


def gathered_sums(values, axis):
    count = lax.axis_size(axis)
    row = values
    spread = jnp.broadcast_to(row[None], (count, row.shape[0]))
    return jnp.sum(lax.all_to_all(spread, axis, 0, 0, tiled=True), axis=0)


def mm(spec, a, b):
    return jnp.einsum(spec, a, b, precision=HIGH)


def left_environment(left_env, maps):
    segments = lax.axis_size("seg")
    segment = lax.axis_index("seg")
    spread = jnp.broadcast_to(maps[None], (segments,) + maps.shape)
    every = lax.all_to_all(spread, "seg", 0, 0, tiled=True)
    width = maps.shape[-1]
    prefix = jnp.broadcast_to(jnp.eye(width, dtype=jnp.float32), maps.shape)
    for step in range(segments - 1):
        grown = mm("kab,kbc->kac", prefix, every[step])
        prefix = jnp.where(step < segment, grown, prefix)
    right_side = mm("wkbc,kcd->wkbd", left_env, prefix)
    return mm("kba,wkbd->wkad", prefix, right_side)


def apply_terms(vector, right, banded, edges):
    group = right.shape[0] // 3
    to_right = mm("ab,wbc->wac", vector[1], right[:group, 1])
    to_left = mm("ab,wbc->wac", vector[0], right[2 * group :, 0])
    from_left = shifted(to_right, "sec", 1)
    from_right = shifted(to_left, "sec", -1)
    products = mm("kab,wkbc->wkac", vector, right)
    inner = mm("kawjb,wjbc->kac", banded, products)
    lower = inner[0] + mm("wab,wbc->ac", edges[0], from_left)
    upper = inner[1] + mm("wab,wbc->ac", edges[1], from_right)
    return jnp.stack([lower, upper], axis=0)


def square_sums(normal, lifted):
    stacked = jnp.stack([normal, lifted, lifted * SHRINK], axis=0)
    return jnp.sum(stacked * stacked, axis=(1, 2, 3))


def scales(sums, cells):
    first = lax.rsqrt(sums[0] / cells + EPS)
    step = first / LIFT
    plain = step * step * sums[1]
    shrunk = jnp.square(step / SHRINK) * sums[2]
    second = lax.rsqrt(jnp.where(jnp.isfinite(sums[1]), plain, shrunk) / cells + EPS)
    return first, second


def per_device(theta_in, left_env, site_maps, right_env, mpo_mask, ranks):
    vector = theta_in[0]
    maps = site_maps[0]
    right = right_env[0]
    blocks = vector.shape[0]
    width = vector.shape[1]
    cells = lax.axis_size("sec") * blocks * width * width
    env = left_environment(left_env, maps)
    weighted = env * mpo_mask.astype(jnp.float32)[:, :, None, None]
    right = jnp.concatenate([right[0::3], right[1::3], right[2::3]], axis=0)
    ordered = jnp.concatenate([weighted[0::3], weighted[1::3], weighted[2::3]], axis=0)
    group = ordered.shape[0] // 3
    shift = jnp.repeat(jnp.arange(-1, 2), group)
    source = jnp.arange(blocks)[:, None, None] + shift[None, :, None]
    keep = (source == jnp.arange(blocks)[None, None, :]).astype(jnp.float32)
    banded = jnp.transpose(ordered, (1, 2, 0, 3))[:, :, :, None, :] * keep[:, None, :, :, None]
    edges = (ordered[:group, 0], ordered[2 * group :, blocks - 1])
    current = apply_terms(vector, right, banded, edges)
    for pair in range(ITERS // 2):
        lifted = apply_terms(current * LIFT, right, banded, edges)
        first, second = scales(gathered_sums(square_sums(current, lifted), "sec"), cells)
        current = lifted * (first / LIFT)
        if 2 * pair + 2 < ITERS:
            current = apply_terms(current * LIFT, right, banded, edges) * (second / LIFT)
        else:
            current = current * second
    rows = lax.broadcasted_iota(jnp.int32, (blocks, width), 1) < ranks[0][:, None]
    trimmed = current * rows.astype(jnp.float32)[:, :, None]
    density = mm("kab,kcb->kac", trimmed, trimmed) / width
    return (current[None], density[None])


def solution(mesh):
    return jax.shard_map(
        per_device,
        mesh=mesh,
        in_specs=(
            P("seg", "sec", None, None),
            P(None, "sec", None, None),
            P("seg", "sec", None, None),
            P("seg", None, "sec", None, None),
            P(None, "sec"),
            P("seg", "sec"),
        ),
        out_specs=(P("seg", "sec", None, None), P("seg", "sec", None, None)),
        check_vma=False,
    )
```

```python
import jax
import jax.numpy as jnp
from jax import lax
from jax.sharding import PartitionSpec as P

ITERS = 4


HIGH = lax.Precision.HIGHEST
EPS = 1e-06
LIFT = 1024.0
SHRINK = 2.0**-50


def shifted(block, axis, step):
    count = lax.axis_size(axis)
    route = [(i, i + step) for i in range(count) if 0 <= i + step < count]
    return lax.ppermute(block, axis, route)


def gathered_sums(values, axis):
    count = lax.axis_size(axis)
    row = values
    spread = jnp.broadcast_to(row[None], (count, row.shape[0]))
    return jnp.sum(lax.all_to_all(spread, axis, 0, 0, tiled=True), axis=0)


def mm(spec, a, b):
    return jnp.einsum(spec, a, b, precision=HIGH)


def left_environment(left_env, maps):
    segments = lax.axis_size("seg")
    segment = lax.axis_index("seg")
    spread = jnp.broadcast_to(maps[None], (segments,) + maps.shape)
    every = lax.all_to_all(spread, "seg", 0, 0, tiled=True)
    width = maps.shape[-1]
    prefix = jnp.broadcast_to(jnp.eye(width, dtype=jnp.float32), maps.shape)
    for step in range(segments - 1):
        grown = mm("kab,kbc->kac", prefix, every[step])
        prefix = jnp.where(step < segment, grown, prefix)
    right_side = mm("wkbc,kcd->wkbd", left_env, prefix)
    return mm("kba,wkbd->wkad", prefix, right_side)


def apply_terms(vector, right, halo, ordered):
    from_left = mm("ab,wbc->wac", shifted(vector[1], "sec", 1), halo[0])
    from_right = mm("ab,wbc->wac", shifted(vector[0], "sec", -1), halo[1])
    products = mm("kab,wkbc->wkac", vector, right)
    lower = jnp.stack([from_left, products[0::3, 0]], axis=1)
    upper = jnp.stack([products[2::3, 1], from_right], axis=1)
    terms = jnp.concatenate([lower, products[1::3], upper], axis=0)
    return mm("wkab,wkbc->kac", ordered, terms)


def square_sums(normal, lifted):
    stacked = jnp.stack([normal, lifted, lifted * SHRINK], axis=0)
    return jnp.sum(stacked * stacked, axis=(1, 2, 3))


def scales(sums, cells):
    first = lax.rsqrt(sums[0] / cells + EPS)
    step = first / LIFT
    plain = step * step * sums[1]
    shrunk = jnp.square(step / SHRINK) * sums[2]
    second = lax.rsqrt(jnp.where(jnp.isfinite(sums[1]), plain, shrunk) / cells + EPS)
    return first, second


def per_device(theta_in, left_env, site_maps, right_env, mpo_mask, ranks):
    vector = theta_in[0]
    maps = site_maps[0]
    right = right_env[0]
    blocks = vector.shape[0]
    width = vector.shape[1]
    cells = lax.axis_size("sec") * blocks * width * width
    env = left_environment(left_env, maps)
    weighted = env * mpo_mask.astype(jnp.float32)[:, :, None, None]
    ordered = jnp.concatenate([weighted[0::3], weighted[1::3], weighted[2::3]], axis=0)
    halo = (shifted(right[0::3, 1], "sec", 1), shifted(right[2::3, 0], "sec", -1))
    current = apply_terms(vector, right, halo, ordered)
    for pair in range(ITERS // 2):
        lifted = apply_terms(current * LIFT, right, halo, ordered)
        first, second = scales(gathered_sums(square_sums(current, lifted), "sec"), cells)
        current = lifted * (first / LIFT)
        if 2 * pair + 2 < ITERS:
            current = apply_terms(current * LIFT, right, halo, ordered) * (second / LIFT)
        else:
            current = current * second
    rows = lax.broadcasted_iota(jnp.int32, (blocks, width), 1) < ranks[0][:, None]
    trimmed = current * rows.astype(jnp.float32)[:, :, None]
    density = mm("kab,kcb->kac", trimmed, trimmed) / width
    return (current[None], density[None])


def solution(mesh):
    return jax.shard_map(
        per_device,
        mesh=mesh,
        in_specs=(
            P("seg", "sec", None, None),
            P(None, "sec", None, None),
            P("seg", "sec", None, None),
            P("seg", None, "sec", None, None),
            P(None, "sec"),
            P("seg", "sec"),
        ),
        out_specs=(P("seg", "sec", None, None), P("seg", "sec", None, None)),
        check_vma=False,
    )
```

```python
import jax
import jax.numpy as jnp
from jax import lax
from jax.sharding import PartitionSpec as P

ITERS = 4


HIGH = lax.Precision.HIGHEST
EPS = 1e-06
LIFT = 1024.0
SHRINK = 2.0**-50


def shifted(block, axis, step):
    count = lax.axis_size(axis)
    route = [(i, i + step) for i in range(count) if 0 <= i + step < count]
    return lax.ppermute(block, axis, route)


def gathered_sums(values, axis):
    count = lax.axis_size(axis)
    row = values
    spread = jnp.broadcast_to(row[None], (count, row.shape[0]))
    return jnp.sum(lax.all_to_all(spread, axis, 0, 0, tiled=True), axis=0)


def mm(spec, a, b):
    return jnp.einsum(spec, a, b, precision=HIGH)


def left_environment(left_env, maps):
    segments = lax.axis_size("seg")
    segment = lax.axis_index("seg")
    spread = jnp.broadcast_to(maps[None], (segments,) + maps.shape)
    every = lax.all_to_all(spread, "seg", 0, 0, tiled=True)
    width = maps.shape[-1]
    prefix = jnp.broadcast_to(jnp.eye(width, dtype=jnp.float32), maps.shape)
    for step in range(segments - 1):
        grown = mm("kab,kbc->kac", prefix, every[step])
        prefix = jnp.where(step < segment, grown, prefix)
    right_side = mm("wkbc,kcd->wkbd", left_env, prefix)
    return mm("kba,wkbd->wkad", prefix, right_side)


def exchange(vector, right):
    products = mm("kab,wkbc->wkac", vector, right)
    from_left = shifted(products[0::3, 1], "sec", 1)
    from_right = shifted(products[2::3, 0], "sec", -1)
    return products, from_left, from_right


def combine(parts, ordered, factor=None):
    products, from_left, from_right = parts
    lower = jnp.stack([from_left, products[0::3, 0]], axis=1)
    upper = jnp.stack([products[2::3, 1], from_right], axis=1)
    terms = jnp.concatenate([lower, products[1::3], upper], axis=0)
    if factor is not None:
        terms = terms * factor
    return mm("wkab,wkbc->kac", ordered, terms)


def apply_terms(vector, right, ordered):
    return combine(exchange(vector, right), ordered)


def square_sums(normal, lifted):
    stacked = jnp.stack([normal, lifted, lifted * SHRINK], axis=0)
    return jnp.sum(stacked * stacked, axis=(1, 2, 3))


def scales(sums, cells):
    first = lax.rsqrt(sums[0] / cells + EPS)
    step = first / LIFT
    plain = step * step * sums[1]
    shrunk = jnp.square(step / SHRINK) * sums[2]
    second = lax.rsqrt(jnp.where(jnp.isfinite(sums[1]), plain, shrunk) / cells + EPS)
    return first, second


def per_device(theta_in, left_env, site_maps, right_env, mpo_mask, ranks):
    vector = theta_in[0]
    maps = site_maps[0]
    right = right_env[0]
    blocks = vector.shape[0]
    width = vector.shape[1]
    cells = lax.axis_size("sec") * blocks * width * width
    env = left_environment(left_env, maps)
    weighted = env * mpo_mask.astype(jnp.float32)[:, :, None, None]
    ordered = jnp.concatenate([weighted[0::3], weighted[1::3], weighted[2::3]], axis=0)
    current = apply_terms(vector, right, ordered)
    for pair in range(ITERS // 2):
        lifted = apply_terms(current * LIFT, right, ordered)
        more = 2 * pair + 2 < ITERS
        if more:
            parts = exchange(lifted * LIFT, right)
        first, second = scales(gathered_sums(square_sums(current, lifted), "sec"), cells)
        if more:
            current = combine(parts, ordered, first / LIFT) * (second / LIFT)
        else:
            current = lifted * (first / LIFT) * second
    rows = lax.broadcasted_iota(jnp.int32, (blocks, width), 1) < ranks[0][:, None]
    trimmed = current * rows.astype(jnp.float32)[:, :, None]
    density = mm("kab,kcb->kac", trimmed, trimmed) / width
    return (current[None], density[None])


def solution(mesh):
    return jax.shard_map(
        per_device,
        mesh=mesh,
        in_specs=(
            P("seg", "sec", None, None),
            P(None, "sec", None, None),
            P("seg", "sec", None, None),
            P("seg", None, "sec", None, None),
            P(None, "sec"),
            P("seg", "sec"),
        ),
        out_specs=(P("seg", "sec", None, None), P("seg", "sec", None, None)),
        check_vma=False,
    )
```

```python
import jax
import jax.numpy as jnp
from jax import lax
from jax.sharding import PartitionSpec as P

ITERS = 4


HIGH = lax.Precision.HIGHEST
EPS = 1e-06
LIFT = 1024.0
SHRINK = 2.0**-50


def shifted(block, axis, step):
    count = lax.axis_size(axis)
    route = [(i, i + step) for i in range(count) if 0 <= i + step < count]
    return lax.ppermute(block, axis, route)


def gathered_sums(values, axis):
    count = lax.axis_size(axis)
    spread = jnp.broadcast_to(values[None, :, None], (count, values.shape[0], 128))
    return jnp.sum(lax.all_to_all(spread, axis, 0, 0, tiled=True), axis=0)


def mm(spec, a, b):
    return jnp.einsum(spec, a, b, precision=HIGH)


def left_environment(left_env, maps):
    segments = lax.axis_size("seg")
    segment = lax.axis_index("seg")
    spread = jnp.broadcast_to(maps[None], (segments,) + maps.shape)
    every = lax.all_to_all(spread, "seg", 0, 0, tiled=True)
    width = maps.shape[-1]
    prefix = jnp.broadcast_to(jnp.eye(width, dtype=jnp.float32), maps.shape)
    for step in range(segments - 1):
        grown = mm("kab,kbc->kac", prefix, every[step])
        prefix = jnp.where(step < segment, grown, prefix)
    right_side = mm("wkbc,kcd->wkbd", left_env, prefix)
    return mm("kba,wkbd->wkad", prefix, right_side)


def exchange(vector, right):
    products = mm("kab,wkbc->wkac", vector, right)
    from_left = shifted(products[0::3, 1], "sec", 1)
    from_right = shifted(products[2::3, 0], "sec", -1)
    return products, from_left, from_right


def combine(parts, ordered, factor=None):
    products, from_left, from_right = parts
    lower = jnp.stack([from_left, products[0::3, 0]], axis=1)
    upper = jnp.stack([products[2::3, 1], from_right], axis=1)
    terms = jnp.concatenate([lower, products[1::3], upper], axis=0)
    if factor is not None:
        terms = terms * factor
    return mm("wkab,wkbc->kac", ordered, terms)


def apply_terms(vector, right, ordered):
    return combine(exchange(vector, right), ordered)


def square_sums(normal, lifted):
    stacked = jnp.stack([normal, lifted, lifted * SHRINK], axis=0)
    return jnp.sum(stacked * stacked, axis=(1, 2, 3))


def scales(sums, cells):
    first = lax.rsqrt(sums[0] / cells + EPS)
    step = first / LIFT
    plain = step * step * sums[1]
    shrunk = jnp.square(step / SHRINK) * sums[2]
    second = lax.rsqrt(jnp.where(jnp.isfinite(sums[1]), plain, shrunk) / cells + EPS)
    return first, second


def per_device(theta_in, left_env, site_maps, right_env, mpo_mask, ranks):
    vector = theta_in[0]
    maps = site_maps[0]
    right = right_env[0]
    blocks = vector.shape[0]
    width = vector.shape[1]
    cells = lax.axis_size("sec") * blocks * width * width
    env = left_environment(left_env, maps)
    weighted = env * mpo_mask.astype(jnp.float32)[:, :, None, None]
    ordered = jnp.concatenate([weighted[0::3], weighted[1::3], weighted[2::3]], axis=0)
    current = apply_terms(vector, right, ordered)
    rows = lax.broadcasted_iota(jnp.int32, (blocks, width), 1) < ranks[0][:, None]
    for pair in range(ITERS // 2):
        lifted = apply_terms(current * LIFT, right, ordered)
        more = 2 * pair + 2 < ITERS
        if more:
            parts = exchange(lifted * LIFT, right)
        else:
            trimmed = lifted * rows.astype(jnp.float32)[:, :, None]
            peak = jnp.maximum(jnp.max(jnp.abs(trimmed)), jnp.finfo(jnp.float32).tiny)
            unit = trimmed * (1.0 / peak)
            gram, peak = lax.optimization_barrier((mm("kab,kcb->kac", unit, unit), peak))
        first, second = scales(gathered_sums(square_sums(current, lifted), "sec"), cells)
        if more:
            current = combine(parts, ordered, first / LIFT) * (second / LIFT)
        else:
            factor = (first / LIFT) * second
            current = lifted * factor
            density = gram * (jnp.square(factor * peak) / width)
    return (current[None], density[None])


def solution(mesh):
    return jax.shard_map(
        per_device,
        mesh=mesh,
        in_specs=(
            P("seg", "sec", None, None),
            P(None, "sec", None, None),
            P("seg", "sec", None, None),
            P("seg", None, "sec", None, None),
            P(None, "sec"),
            P("seg", "sec"),
        ),
        out_specs=(P("seg", "sec", None, None), P("seg", "sec", None, None)),
        check_vma=False,
    )
```

```python
import jax
import jax.numpy as jnp
from jax import lax
from jax.sharding import PartitionSpec as P

ITERS = 4


HIGH = lax.Precision.HIGH
EPS = 1e-06
LIFT = 1024.0
SHRINK = 2.0**-50


def shifted(block, axis, step):
    count = lax.axis_size(axis)
    route = [(i, i + step) for i in range(count) if 0 <= i + step < count]
    return lax.ppermute(block, axis, route)


def gathered_sums(values, axis):
    count = lax.axis_size(axis)
    spread = jnp.broadcast_to(values[None, :, None], (count, values.shape[0], 128))
    return jnp.sum(lax.all_to_all(spread, axis, 0, 0, tiled=True), axis=0)


def mm(spec, a, b):
    return jnp.einsum(spec, a, b, precision=HIGH)


def left_environment(left_env, maps):
    segments = lax.axis_size("seg")
    segment = lax.axis_index("seg")
    spread = jnp.broadcast_to(maps[None], (segments,) + maps.shape)
    every = lax.all_to_all(spread, "seg", 0, 0, tiled=True)
    width = maps.shape[-1]
    prefix = jnp.broadcast_to(jnp.eye(width, dtype=jnp.float32), maps.shape)
    for step in range(segments - 1):
        grown = mm("kab,kbc->kac", prefix, every[step])
        prefix = jnp.where(step < segment, grown, prefix)
    right_side = mm("wkbc,kcd->wkbd", left_env, prefix)
    return mm("kba,wkbd->wkad", prefix, right_side)


def exchange(vector, right):
    products = mm("kab,wkbc->wkac", vector, right)
    from_left = shifted(products[0::3, 1], "sec", 1)
    from_right = shifted(products[2::3, 0], "sec", -1)
    return products, from_left, from_right


def combine(parts, ordered, factor=None):
    products, from_left, from_right = parts
    lower = jnp.stack([from_left, products[0::3, 0]], axis=1)
    upper = jnp.stack([products[2::3, 1], from_right], axis=1)
    terms = jnp.concatenate([lower, products[1::3], upper], axis=0)
    if factor is not None:
        terms = terms * factor
    return mm("wkab,wkbc->kac", ordered, terms)


def apply_terms(vector, right, ordered):
    return combine(exchange(vector, right), ordered)


def square_sums(normal, lifted):
    stacked = jnp.stack([normal, lifted, lifted * SHRINK], axis=0)
    return jnp.sum(stacked * stacked, axis=(1, 2, 3))


def scales(sums, cells):
    first = lax.rsqrt(sums[0] / cells + EPS)
    step = first / LIFT
    plain = step * step * sums[1]
    shrunk = jnp.square(step / SHRINK) * sums[2]
    second = lax.rsqrt(jnp.where(jnp.isfinite(sums[1]), plain, shrunk) / cells + EPS)
    return first, second


def per_device(theta_in, left_env, site_maps, right_env, mpo_mask, ranks):
    vector = theta_in[0]
    maps = site_maps[0]
    right = right_env[0]
    blocks = vector.shape[0]
    width = vector.shape[1]
    cells = lax.axis_size("sec") * blocks * width * width
    env = left_environment(left_env, maps)
    weighted = env * mpo_mask.astype(jnp.float32)[:, :, None, None]
    ordered = jnp.concatenate([weighted[0::3], weighted[1::3], weighted[2::3]], axis=0)
    current = apply_terms(vector, right, ordered)
    rows = lax.broadcasted_iota(jnp.int32, (blocks, width), 1) < ranks[0][:, None]
    for pair in range(ITERS // 2):
        lifted = apply_terms(current * LIFT, right, ordered)
        more = 2 * pair + 2 < ITERS
        if more:
            parts = exchange(lifted * LIFT, right)
        else:
            trimmed = lifted * rows.astype(jnp.float32)[:, :, None]
            peak = jnp.maximum(jnp.max(jnp.abs(trimmed)), jnp.finfo(jnp.float32).tiny)
            unit = trimmed * (1.0 / peak)
            gram, peak = lax.optimization_barrier((mm("kab,kcb->kac", unit, unit), peak))
        first, second = scales(gathered_sums(square_sums(current, lifted), "sec"), cells)
        if more:
            current = combine(parts, ordered, first / LIFT) * (second / LIFT)
        else:
            factor = (first / LIFT) * second
            current = lifted * factor
            density = gram * (jnp.square(factor * peak) / width)
    return (current[None], density[None])


def solution(mesh):
    return jax.shard_map(
        per_device,
        mesh=mesh,
        in_specs=(
            P("seg", "sec", None, None),
            P(None, "sec", None, None),
            P("seg", "sec", None, None),
            P("seg", None, "sec", None, None),
            P(None, "sec"),
            P("seg", "sec"),
        ),
        out_specs=(P("seg", "sec", None, None), P("seg", "sec", None, None)),
        check_vma=False,
    )
```

```python
import jax
import jax.numpy as jnp
from jax import lax
from jax.sharding import PartitionSpec as P

ITERS = 4


HIGH = lax.Precision.HIGH
EXACT = lax.Precision.HIGHEST
EPS = 1e-06
LIFT = 1024.0
SHRINK = 2.0**-50


def shifted(block, axis, step):
    count = lax.axis_size(axis)
    route = [(i, i + step) for i in range(count) if 0 <= i + step < count]
    return lax.ppermute(block, axis, route)


def gathered_sums(values, axis):
    count = lax.axis_size(axis)
    spread = jnp.broadcast_to(values[None, :, None], (count, values.shape[0], 128))
    return jnp.sum(lax.all_to_all(spread, axis, 0, 0, tiled=True), axis=0)


def mm(spec, a, b, precision=HIGH):
    return jnp.einsum(spec, a, b, precision=precision)


def left_environment(left_env, maps):
    segments = lax.axis_size("seg")
    segment = lax.axis_index("seg")
    spread = jnp.broadcast_to(maps[None], (segments,) + maps.shape)
    every = lax.all_to_all(spread, "seg", 0, 0, tiled=True)
    width = maps.shape[-1]
    prefix = jnp.broadcast_to(jnp.eye(width, dtype=jnp.float32), maps.shape)
    for step in range(segments - 1):
        grown = mm("kab,kbc->kac", prefix, every[step], EXACT)
        prefix = jnp.where(step < segment, grown, prefix)
    right_side = mm("wkbc,kcd->wkbd", left_env, prefix, EXACT)
    return mm("kba,wkbd->wkad", prefix, right_side, EXACT)


def exchange(vector, right):
    products = mm("kab,wkbc->wkac", vector, right)
    from_left = shifted(products[0::3, 1], "sec", 1)
    from_right = shifted(products[2::3, 0], "sec", -1)
    return products, from_left, from_right


def combine(parts, ordered, factor=None):
    products, from_left, from_right = parts
    lower = jnp.stack([from_left, products[0::3, 0]], axis=1)
    upper = jnp.stack([products[2::3, 1], from_right], axis=1)
    terms = jnp.concatenate([lower, products[1::3], upper], axis=0)
    if factor is not None:
        terms = terms * factor
    return mm("wkab,wkbc->kac", ordered, terms)


def apply_terms(vector, right, ordered):
    return combine(exchange(vector, right), ordered)


def square_sums(normal, lifted):
    stacked = jnp.stack([normal, lifted, lifted * SHRINK], axis=0)
    return jnp.sum(stacked * stacked, axis=(1, 2, 3))


def scales(sums, cells):
    first = lax.rsqrt(sums[0] / cells + EPS)
    step = first / LIFT
    plain = step * step * sums[1]
    shrunk = jnp.square(step / SHRINK) * sums[2]
    second = lax.rsqrt(jnp.where(jnp.isfinite(sums[1]), plain, shrunk) / cells + EPS)
    return first, second


def per_device(theta_in, left_env, site_maps, right_env, mpo_mask, ranks):
    vector = theta_in[0]
    maps = site_maps[0]
    right = right_env[0]
    blocks = vector.shape[0]
    width = vector.shape[1]
    cells = lax.axis_size("sec") * blocks * width * width
    env = left_environment(left_env, maps)
    weighted = env * mpo_mask.astype(jnp.float32)[:, :, None, None]
    ordered = jnp.concatenate([weighted[0::3], weighted[1::3], weighted[2::3]], axis=0)
    current = apply_terms(vector, right, ordered)
    rows = lax.broadcasted_iota(jnp.int32, (blocks, width), 1) < ranks[0][:, None]
    for pair in range(ITERS // 2):
        lifted = apply_terms(current * LIFT, right, ordered)
        more = 2 * pair + 2 < ITERS
        if more:
            parts = exchange(lifted * LIFT, right)
        else:
            trimmed = lifted * rows.astype(jnp.float32)[:, :, None]
            peak = jnp.maximum(jnp.max(jnp.abs(trimmed)), jnp.finfo(jnp.float32).tiny)
            unit = trimmed * (1.0 / peak)
            gram, peak = lax.optimization_barrier((mm("kab,kcb->kac", unit, unit), peak))
        first, second = scales(gathered_sums(square_sums(current, lifted), "sec"), cells)
        if more:
            current = combine(parts, ordered, first / LIFT) * (second / LIFT)
        else:
            factor = (first / LIFT) * second
            current = lifted * factor
            density = gram * (jnp.square(factor * peak) / width)
    return (current[None], density[None])


def solution(mesh):
    return jax.shard_map(
        per_device,
        mesh=mesh,
        in_specs=(
            P("seg", "sec", None, None),
            P(None, "sec", None, None),
            P("seg", "sec", None, None),
            P("seg", None, "sec", None, None),
            P(None, "sec"),
            P("seg", "sec"),
        ),
        out_specs=(P("seg", "sec", None, None), P("seg", "sec", None, None)),
        check_vma=False,
    )
```

```python
import jax
import jax.numpy as jnp
from jax import lax
from jax.sharding import PartitionSpec as P

ITERS = 4


HIGH = lax.Precision.HIGH
EXACT = lax.Precision.HIGHEST
EPS = 1e-06
LIFT = 1024.0
SHRINK = 2.0**-50


def shifted(block, axis, step):
    count = lax.axis_size(axis)
    route = [(i, i + step) for i in range(count) if 0 <= i + step < count]
    return lax.ppermute(block, axis, route)


def gathered_sums(values, axis):
    count = lax.axis_size(axis)
    spread = jnp.broadcast_to(values[None, :, None], (count, values.shape[0], 128))
    return jnp.sum(lax.all_to_all(spread, axis, 0, 0, tiled=True), axis=0)


def mm(spec, a, b, precision=HIGH):
    return jnp.einsum(spec, a, b, precision=precision)


def left_environment(left_env, maps):
    segments = lax.axis_size("seg")
    segment = lax.axis_index("seg")
    spread = jnp.broadcast_to(maps[None], (segments,) + maps.shape)
    every = lax.all_to_all(spread, "seg", 0, 0, tiled=True)
    scan = every[: segments - 1]
    reach = 1
    while reach < segments - 1:
        joined = mm("tkab,tkbc->tkac", scan[:-reach], scan[reach:], EXACT)
        scan = jnp.concatenate([scan[:reach], joined], axis=0)
        reach *= 2
    width = maps.shape[-1]
    eye = jnp.broadcast_to(jnp.eye(width, dtype=jnp.float32), maps.shape)
    before = lax.dynamic_index_in_dim(scan, jnp.maximum(segment - 1, 0), 0, keepdims=False)
    prefix = jnp.where(segment > 0, before, eye)
    right_side = mm("wkbc,kcd->wkbd", left_env, prefix, EXACT)
    return mm("kba,wkbd->wkad", prefix, right_side, EXACT)


def exchange(vector, right):
    products = mm("kab,wkbc->wkac", vector, right)
    from_left = shifted(mm("ab,wbc->wac", vector[1], right[0::3, 1]), "sec", 1)
    from_right = shifted(mm("ab,wbc->wac", vector[0], right[2::3, 0]), "sec", -1)
    return products, from_left, from_right


def combine(parts, ordered, factor=None):
    products, from_left, from_right = parts
    lower = jnp.stack([from_left, products[0::3, 0]], axis=1)
    upper = jnp.stack([products[2::3, 1], from_right], axis=1)
    terms = jnp.concatenate([lower, products[1::3], upper], axis=0)
    if factor is not None:
        terms = terms * factor
    return mm("wkab,wkbc->kac", ordered, terms)


def apply_terms(vector, right, ordered):
    products = mm("kab,wkbc->wkac", vector, right)
    from_left = shifted(products[0::3, 1], "sec", 1)
    from_right = shifted(products[2::3, 0], "sec", -1)
    return combine((products, from_left, from_right), ordered)


def square_sums(normal, lifted):
    stacked = jnp.stack([normal, lifted, lifted * SHRINK], axis=0)
    return jnp.sum(stacked * stacked, axis=(1, 2, 3))


def scales(sums, cells):
    first = lax.rsqrt(sums[0] / cells + EPS)
    step = first / LIFT
    plain = step * step * sums[1]
    shrunk = jnp.square(step / SHRINK) * sums[2]
    second = lax.rsqrt(jnp.where(jnp.isfinite(sums[1]), plain, shrunk) / cells + EPS)
    return first, second


def per_device(theta_in, left_env, site_maps, right_env, mpo_mask, ranks):
    vector = theta_in[0]
    maps = site_maps[0]
    right = right_env[0]
    blocks = vector.shape[0]
    width = vector.shape[1]
    cells = lax.axis_size("sec") * blocks * width * width
    env = left_environment(left_env, maps)
    weighted = env * mpo_mask.astype(jnp.float32)[:, :, None, None]
    ordered = jnp.concatenate([weighted[0::3], weighted[1::3], weighted[2::3]], axis=0)
    current = apply_terms(vector, right, ordered)
    rows = lax.broadcasted_iota(jnp.int32, (blocks, width), 1) < ranks[0][:, None]
    for pair in range(ITERS // 2):
        lifted = apply_terms(current * LIFT, right, ordered)
        more = 2 * pair + 2 < ITERS
        if more:
            parts = exchange(lifted * LIFT, right)
        else:
            trimmed = lifted * rows.astype(jnp.float32)[:, :, None]
            peak = jnp.maximum(jnp.max(jnp.abs(trimmed)), jnp.finfo(jnp.float32).tiny)
            unit = trimmed * (1.0 / peak)
            gram, peak = lax.optimization_barrier((mm("kab,kcb->kac", unit, unit), peak))
        first, second = scales(gathered_sums(square_sums(current, lifted), "sec"), cells)
        if more:
            current = combine(parts, ordered, first / LIFT) * (second / LIFT)
        else:
            factor = (first / LIFT) * second
            current = lifted * factor
            density = gram * (jnp.square(factor * peak) / width)
    return (current[None], density[None])


def solution(mesh):
    return jax.shard_map(
        per_device,
        mesh=mesh,
        in_specs=(
            P("seg", "sec", None, None),
            P(None, "sec", None, None),
            P("seg", "sec", None, None),
            P("seg", None, "sec", None, None),
            P(None, "sec"),
            P("seg", "sec"),
        ),
        out_specs=(P("seg", "sec", None, None), P("seg", "sec", None, None)),
        check_vma=False,
    )
```

```python
import jax
import jax.numpy as jnp
from jax import lax
from jax.sharding import PartitionSpec as P

ITERS = 4


HIGH = lax.Precision.HIGH
EXACT = lax.Precision.HIGHEST
EPS = 1e-06
LIFT = 1024.0
SHRINK = 2.0**-50


def shifted(block, axis, step):
    count = lax.axis_size(axis)
    route = [(i, i + step) for i in range(count) if 0 <= i + step < count]
    return lax.ppermute(block, axis, route)


def gathered_sums(values, axis):
    count = lax.axis_size(axis)
    spread = jnp.broadcast_to(values[None, :, None], (count, values.shape[0], 128))
    return jnp.sum(lax.all_to_all(spread, axis, 0, 0, tiled=True), axis=0)


def mm(spec, a, b, precision=HIGH):
    return jnp.einsum(spec, a, b, precision=precision)


def left_environment(left_env, maps):
    segments = lax.axis_size("seg")
    segment = lax.axis_index("seg")
    spread = jnp.broadcast_to(maps[None], (segments,) + maps.shape)
    every = lax.all_to_all(spread, "seg", 0, 0, tiled=True)
    width = maps.shape[-1]
    prefix = jnp.broadcast_to(jnp.eye(width, dtype=jnp.float32), maps.shape)
    for step in range(segments - 1):
        grown = mm("kab,kbc->kac", prefix, every[step], EXACT)
        prefix = jnp.where(step < segment, grown, prefix)
    right_side = mm("wkbc,kcd->wkbd", left_env, prefix)
    return mm("kba,wkbd->wkad", prefix, right_side)


def exchange(vector, right):
    products = mm("kab,wkbc->wkac", vector, right)
    from_left = shifted(products[0::3, 1], "sec", 1)
    from_right = shifted(products[2::3, 0], "sec", -1)
    return products, from_left, from_right


def combine(parts, ordered):
    products, from_left, from_right = parts
    lower = jnp.stack([from_left, products[0::3, 0]], axis=1)
    upper = jnp.stack([products[2::3, 1], from_right], axis=1)
    terms = jnp.concatenate([lower, products[1::3], upper], axis=0)
    return mm("wkab,wkbc->kac", ordered, terms)


def apply_terms(vector, right, ordered):
    return combine(exchange(vector, right), ordered)


def square_sums(normal, lifted):
    stacked = jnp.stack([normal, lifted, lifted * SHRINK], axis=0)
    return jnp.sum(stacked * stacked, axis=(1, 2, 3))


def scales(sums, cells):
    first = lax.rsqrt(sums[0] / cells + EPS)
    step = first / LIFT
    plain = step * step * sums[1]
    shrunk = jnp.square(step / SHRINK) * sums[2]
    second = lax.rsqrt(jnp.where(jnp.isfinite(sums[1]), plain, shrunk) / cells + EPS)
    return first, second


def per_device(theta_in, left_env, site_maps, right_env, mpo_mask, ranks):
    vector = theta_in[0]
    maps = site_maps[0]
    right = right_env[0]
    blocks = vector.shape[0]
    width = vector.shape[1]
    cells = lax.axis_size("sec") * blocks * width * width
    env = left_environment(left_env, maps)
    weighted = env * mpo_mask.astype(jnp.float32)[:, :, None, None]
    ordered = jnp.concatenate([weighted[0::3], weighted[1::3], weighted[2::3]], axis=0)
    current = apply_terms(vector, right, ordered)
    rows = lax.broadcasted_iota(jnp.int32, (blocks, width), 1) < ranks[0][:, None]
    for pair in range(ITERS // 2):
        lifted = apply_terms(current * LIFT, right, ordered)
        more = 2 * pair + 2 < ITERS
        if more:
            parts = exchange(lifted * LIFT, right)
        else:
            trimmed = lifted * rows.astype(jnp.float32)[:, :, None]
            peak = jnp.maximum(jnp.max(jnp.abs(trimmed)), jnp.finfo(jnp.float32).tiny)
            unit = trimmed * (1.0 / peak)
            gram, peak = lax.optimization_barrier((mm("kab,kcb->kac", unit, unit), peak))
        first, second = scales(gathered_sums(square_sums(current, lifted), "sec"), cells)
        if more:
            current = combine(parts, ordered * (first / LIFT)) * (second / LIFT)
        else:
            factor = (first / LIFT) * second
            current = lifted * factor
            density = gram * (jnp.square(factor * peak) / width)
    return (current[None], density[None])


def solution(mesh):
    return jax.shard_map(
        per_device,
        mesh=mesh,
        in_specs=(
            P("seg", "sec", None, None),
            P(None, "sec", None, None),
            P("seg", "sec", None, None),
            P("seg", None, "sec", None, None),
            P(None, "sec"),
            P("seg", "sec"),
        ),
        out_specs=(P("seg", "sec", None, None), P("seg", "sec", None, None)),
        check_vma=False,
    )
```

```python
import jax
import jax.numpy as jnp
from jax import lax
from jax.sharding import PartitionSpec as P

ITERS = 4


HIGH = lax.Precision.HIGH
EXACT = lax.Precision.HIGHEST
EPS = 1e-06
LIFT = 1024.0
SHRINK = 2.0**-50


def shifted(block, axis, step):
    count = lax.axis_size(axis)
    route = [(i, i + step) for i in range(count) if 0 <= i + step < count]
    return lax.ppermute(block, axis, route)


def gathered_sums(values, axis):
    count = lax.axis_size(axis)
    spread = jnp.broadcast_to(values[None, :, None], (count, values.shape[0], 128))
    return jnp.sum(lax.all_to_all(spread, axis, 0, 0, tiled=True), axis=0)


def mm(spec, a, b, precision=HIGH):
    return jnp.einsum(spec, a, b, precision=precision)


def prefix_products(maps):
    segments = lax.axis_size("seg")
    segment = lax.axis_index("seg")
    spread = jnp.broadcast_to(maps[None], (segments,) + maps.shape)
    every = lax.all_to_all(spread, "seg", 0, 0, tiled=True)
    width = maps.shape[-1]
    prefix = jnp.broadcast_to(jnp.eye(width, dtype=jnp.float32), maps.shape)
    for step in range(segments - 1):
        grown = mm("kab,kbc->kac", prefix, every[step], EXACT)
        prefix = jnp.where(step < segment, grown, prefix)
    return prefix


def sandwich(prefix, terms):
    return mm("kba,wkbd->wkad", prefix, mm("wkbc,kcd->wkbd", terms, prefix))


def exchange(vector, right):
    products = mm("kab,wkbc->wkac", vector, right)
    from_left = shifted(products[0::3, 1], "sec", 1)
    from_right = shifted(products[2::3, 0], "sec", -1)
    return products, from_left, from_right


def gathered(parts):
    products, from_left, from_right = parts
    lower = jnp.stack([from_left, products[0::3, 0]], axis=1)
    upper = jnp.stack([products[2::3, 1], from_right], axis=1)
    return jnp.concatenate([lower, products[1::3], upper], axis=0)


def combine(parts, ordered):
    return mm("wkab,wkbc->kac", ordered, gathered(parts))


def apply_terms(vector, right, ordered):
    return combine(exchange(vector, right), ordered)


def square_sums(normal, lifted):
    stacked = jnp.stack([normal, lifted, lifted * SHRINK], axis=0)
    return jnp.sum(stacked * stacked, axis=(1, 2, 3))


def scales(sums, cells):
    first = lax.rsqrt(sums[0] / cells + EPS)
    step = first / LIFT
    plain = step * step * sums[1]
    shrunk = jnp.square(step / SHRINK) * sums[2]
    second = lax.rsqrt(jnp.where(jnp.isfinite(sums[1]), plain, shrunk) / cells + EPS)
    return first, second


def per_device(theta_in, left_env, site_maps, right_env, mpo_mask, ranks):
    vector = theta_in[0]
    maps = site_maps[0]
    right = right_env[0]
    blocks = vector.shape[0]
    width = vector.shape[1]
    cells = lax.axis_size("sec") * blocks * width * width
    prefix = prefix_products(maps)
    masked = left_env * mpo_mask.astype(jnp.float32)[:, :, None, None]
    start = jnp.concatenate([masked[0::3], masked[1::3], masked[2::3]], axis=0)
    parts = exchange(vector, right)
    moved = mm("kab,wkbc->wkac", prefix, gathered(parts))
    current = mm("kba,kbc->kac", prefix, mm("wkab,wkbc->kac", start, moved))
    ordered = sandwich(prefix, start)
    rows = lax.broadcasted_iota(jnp.int32, (blocks, width), 1) < ranks[0][:, None]
    for pair in range(ITERS // 2):
        lifted = apply_terms(current * LIFT, right, ordered)
        more = 2 * pair + 2 < ITERS
        if more:
            parts = exchange(lifted * LIFT, right)
        else:
            trimmed = lifted * rows.astype(jnp.float32)[:, :, None]
            peak = jnp.maximum(jnp.max(jnp.abs(trimmed)), jnp.finfo(jnp.float32).tiny)
            unit = trimmed * (1.0 / peak)
            gram, peak = lax.optimization_barrier((mm("kab,kcb->kac", unit, unit), peak))
        first, second = scales(gathered_sums(square_sums(current, lifted), "sec"), cells)
        if more:
            current = combine(parts, ordered * (first / LIFT)) * (second / LIFT)
        else:
            factor = (first / LIFT) * second
            current = lifted * factor
            density = gram * (jnp.square(factor * peak) / width)
    return (current[None], density[None])


def solution(mesh):
    return jax.shard_map(
        per_device,
        mesh=mesh,
        in_specs=(
            P("seg", "sec", None, None),
            P(None, "sec", None, None),
            P("seg", "sec", None, None),
            P("seg", None, "sec", None, None),
            P(None, "sec"),
            P("seg", "sec"),
        ),
        out_specs=(P("seg", "sec", None, None), P("seg", "sec", None, None)),
        check_vma=False,
    )
```

```python
import jax
import jax.numpy as jnp
from jax import lax
from jax.sharding import PartitionSpec as P

ITERS = 4


HIGH = lax.Precision.HIGH
EXACT = lax.Precision.HIGHEST
EPS = 1e-06
LIFT = 1024.0
SHRINK = 2.0**-50


def shifted(block, axis, step):
    count = lax.axis_size(axis)
    route = [(i, i + step) for i in range(count) if 0 <= i + step < count]
    return lax.ppermute(block, axis, route)


def gathered_sums(values, axis):
    count = lax.axis_size(axis)
    spread = jnp.broadcast_to(values[None, :, None], (count, values.shape[0], 128))
    return jnp.sum(lax.all_to_all(spread, axis, 0, 0, tiled=True), axis=0)


def mm(spec, a, b, precision=HIGH):
    return jnp.einsum(spec, a, b, precision=precision)


def left_environment(left_env, maps):
    segments = lax.axis_size("seg")
    segment = lax.axis_index("seg")
    spread = jnp.broadcast_to(maps[None], (segments,) + maps.shape)
    every = lax.all_to_all(spread, "seg", 0, 0, tiled=True)
    width = maps.shape[-1]
    prefix = jnp.broadcast_to(jnp.eye(width, dtype=jnp.float32), maps.shape)
    for step in range(segments - 1):
        grown = mm("kab,kbc->kac", prefix, every[step], EXACT)
        prefix = jnp.where(step < segment, grown, prefix)
    right_side = mm("wkbc,kcd->wkbd", left_env, prefix)
    return mm("kba,wkbd->wkad", prefix, right_side)


def exchange(vector, right):
    products = mm("kab,wkbc->wkac", vector, right)
    from_left = shifted(products[0::3, 1], "sec", 1)
    from_right = shifted(products[2::3, 0], "sec", -1)
    return products, from_left, from_right


def combine(parts, ordered):
    products, from_left, from_right = parts
    lower = jnp.stack([from_left, products[0::3, 0]], axis=1)
    upper = jnp.stack([products[2::3, 1], from_right], axis=1)
    terms = jnp.concatenate([lower, products[1::3], upper], axis=0)
    return mm("wkab,wkbc->kac", ordered, terms)


def apply_terms(vector, right, ordered, split=False):
    if not split:
        return combine(exchange(vector, right), ordered)
    products, from_left, from_right = exchange(vector, right)
    group = ordered.shape[0] // 3
    blank = jnp.zeros_like(from_left)
    inner = combine((products, blank, blank), ordered)
    lower = inner[0] + mm("wab,wbc->ac", ordered[:group, 0], from_left)
    upper = inner[1] + mm("wab,wbc->ac", ordered[2 * group :, 1], from_right)
    return jnp.stack([lower, upper], axis=0)


def square_sums(normal, lifted):
    stacked = jnp.stack([normal, lifted, lifted * SHRINK], axis=0)
    return jnp.sum(stacked * stacked, axis=(1, 2, 3))


def scales(sums, cells):
    first = lax.rsqrt(sums[0] / cells + EPS)
    step = first / LIFT
    plain = step * step * sums[1]
    shrunk = jnp.square(step / SHRINK) * sums[2]
    second = lax.rsqrt(jnp.where(jnp.isfinite(sums[1]), plain, shrunk) / cells + EPS)
    return first, second


def per_device(theta_in, left_env, site_maps, right_env, mpo_mask, ranks):
    vector = theta_in[0]
    maps = site_maps[0]
    right = right_env[0]
    blocks = vector.shape[0]
    width = vector.shape[1]
    cells = lax.axis_size("sec") * blocks * width * width
    env = left_environment(left_env, maps)
    weighted = env * mpo_mask.astype(jnp.float32)[:, :, None, None]
    ordered = jnp.concatenate([weighted[0::3], weighted[1::3], weighted[2::3]], axis=0)
    current = apply_terms(vector, right, ordered)
    rows = lax.broadcasted_iota(jnp.int32, (blocks, width), 1) < ranks[0][:, None]
    for pair in range(ITERS // 2):
        lifted = apply_terms(current * LIFT, right, ordered, split=True)
        more = 2 * pair + 2 < ITERS
        if more:
            parts = exchange(lifted * LIFT, right)
        else:
            trimmed = lifted * rows.astype(jnp.float32)[:, :, None]
            peak = jnp.maximum(jnp.max(jnp.abs(trimmed)), jnp.finfo(jnp.float32).tiny)
            unit = trimmed * (1.0 / peak)
            gram, peak = lax.optimization_barrier((mm("kab,kcb->kac", unit, unit), peak))
        first, second = scales(gathered_sums(square_sums(current, lifted), "sec"), cells)
        if more:
            current = combine(parts, ordered * (first / LIFT)) * (second / LIFT)
        else:
            factor = (first / LIFT) * second
            current = lifted * factor
            density = gram * (jnp.square(factor * peak) / width)
    return (current[None], density[None])


def solution(mesh):
    return jax.shard_map(
        per_device,
        mesh=mesh,
        in_specs=(
            P("seg", "sec", None, None),
            P(None, "sec", None, None),
            P("seg", "sec", None, None),
            P("seg", None, "sec", None, None),
            P(None, "sec"),
            P("seg", "sec"),
        ),
        out_specs=(P("seg", "sec", None, None), P("seg", "sec", None, None)),
        check_vma=False,
    )
```

```python
import jax
import jax.numpy as jnp
from jax import lax
from jax.sharding import PartitionSpec as P

ITERS = 4


HIGH = lax.Precision.HIGH
EXACT = lax.Precision.HIGHEST
EPS = 1e-06
LIFT = 1024.0
SHRINK = 2.0**-50


def shifted(block, axis, step):
    count = lax.axis_size(axis)
    route = [(i, i + step) for i in range(count) if 0 <= i + step < count]
    return lax.ppermute(block, axis, route)


def gathered_sums(values, axis):
    count = lax.axis_size(axis)
    spread = jnp.broadcast_to(values[None, :, None], (count, values.shape[0], 128))
    return jnp.sum(lax.all_to_all(spread, axis, 0, 0, tiled=True), axis=0)


def mm(spec, a, b, precision=HIGH):
    return jnp.einsum(spec, a, b, precision=precision)


def left_environment(left_env, maps):
    segments = lax.axis_size("seg")
    segment = lax.axis_index("seg")
    spread = jnp.broadcast_to(maps[None], (segments,) + maps.shape)
    every = lax.all_to_all(spread, "seg", 0, 0, tiled=True)
    width = maps.shape[-1]
    prefix = jnp.broadcast_to(jnp.eye(width, dtype=jnp.float32), maps.shape)
    for step in range(segments - 1):
        grown = mm("kab,kbc->kac", prefix, every[step], EXACT)
        prefix = jnp.where(step < segment, grown, prefix)
    right_side = mm("wkbc,kcd->wkbd", left_env, prefix)
    return mm("kba,wkbd->wkad", prefix, right_side)


def exchange(vector, right):
    products = mm("kab,wkbc->wkac", vector, right)
    from_left = shifted(products[0::3, 1], "sec", 1)
    from_right = shifted(products[2::3, 0], "sec", -1)
    return products, from_left, from_right


def combine(parts, ordered):
    products, from_left, from_right = parts
    lower = jnp.stack([from_left, products[0::3, 0]], axis=1)
    upper = jnp.stack([products[2::3, 1], from_right], axis=1)
    terms = jnp.concatenate([lower, products[1::3], upper], axis=0)
    return mm("wkab,wkbc->kac", ordered, terms)


def split_image(parts, ordered):
    products, from_left, from_right = parts
    group = ordered.shape[0] // 3
    blank = jnp.zeros_like(from_left)
    inner = combine((products, blank, blank), ordered)
    lower = inner[0] + mm("wab,wbc->ac", ordered[:group, 0], from_left)
    upper = inner[1] + mm("wab,wbc->ac", ordered[2 * group :, 1], from_right)
    return jnp.stack([lower, upper], axis=0)


def apply_terms(vector, right, ordered, split=False):
    if not split:
        return combine(exchange(vector, right), ordered)
    return split_image(exchange(vector, right), ordered)


def square_sums(normal, lifted):
    stacked = jnp.stack([normal, lifted, lifted * SHRINK], axis=0)
    return jnp.sum(stacked * stacked, axis=(1, 2, 3))


def scales(sums, cells):
    first = lax.rsqrt(sums[0] / cells + EPS)
    step = first / LIFT
    plain = step * step * sums[1]
    shrunk = jnp.square(step / SHRINK) * sums[2]
    second = lax.rsqrt(jnp.where(jnp.isfinite(sums[1]), plain, shrunk) / cells + EPS)
    return first, second


def per_device(theta_in, left_env, site_maps, right_env, mpo_mask, ranks):
    vector = theta_in[0]
    maps = site_maps[0]
    right = right_env[0]
    blocks = vector.shape[0]
    width = vector.shape[1]
    cells = lax.axis_size("sec") * blocks * width * width
    env = left_environment(left_env, maps)
    weighted = env * mpo_mask.astype(jnp.float32)[:, :, None, None]
    ordered = jnp.concatenate([weighted[0::3], weighted[1::3], weighted[2::3]], axis=0)
    current = apply_terms(vector, right, ordered)
    rows = lax.broadcasted_iota(jnp.int32, (blocks, width), 1) < ranks[0][:, None]
    for pair in range(ITERS // 2):
        lifted = apply_terms(current * LIFT, right, ordered, split=True)
        more = 2 * pair + 2 < ITERS
        if more:
            parts = exchange(lifted * LIFT, right)
        else:
            trimmed = lifted * rows.astype(jnp.float32)[:, :, None]
            peak = jnp.maximum(jnp.max(jnp.abs(trimmed)), jnp.finfo(jnp.float32).tiny)
            unit = trimmed * (1.0 / peak)
            gram, peak = lax.optimization_barrier((mm("kab,kcb->kac", unit, unit), peak))
        first, second = scales(gathered_sums(square_sums(current, lifted), "sec"), cells)
        if more:
            current = split_image(parts, ordered * (first / LIFT)) * (second / LIFT)
        else:
            factor = (first / LIFT) * second
            current = lifted * factor
            density = gram * (jnp.square(factor * peak) / width)
    return (current[None], density[None])


def solution(mesh):
    return jax.shard_map(
        per_device,
        mesh=mesh,
        in_specs=(
            P("seg", "sec", None, None),
            P(None, "sec", None, None),
            P("seg", "sec", None, None),
            P("seg", None, "sec", None, None),
            P(None, "sec"),
            P("seg", "sec"),
        ),
        out_specs=(P("seg", "sec", None, None), P("seg", "sec", None, None)),
        check_vma=False,
    )
```

```python
import jax
import jax.numpy as jnp
from jax import lax
from jax.sharding import PartitionSpec as P

ITERS = 4


HIGH = lax.Precision.HIGH
EXACT = lax.Precision.HIGHEST
EPS = 1e-06
LIFT = 1024.0
SHRINK = 2.0**-50


def shifted(block, axis, step):
    count = lax.axis_size(axis)
    route = [(i, i + step) for i in range(count) if 0 <= i + step < count]
    return lax.ppermute(block, axis, route)


def gathered_sums(values, axis):
    count = lax.axis_size(axis)
    rows = jnp.concatenate([values, jnp.zeros((8 - values.shape[0],), values.dtype)])
    spread = jnp.broadcast_to(rows[None, :, None], (count, 8, 128))
    return jnp.sum(lax.all_to_all(spread, axis, 0, 0, tiled=True), axis=0)[: values.shape[0]]


def mm(spec, a, b, precision=HIGH):
    return jnp.einsum(spec, a, b, precision=precision)


def left_environment(left_env, maps):
    segments = lax.axis_size("seg")
    segment = lax.axis_index("seg")
    spread = jnp.broadcast_to(maps[None], (segments,) + maps.shape)
    every = lax.all_to_all(spread, "seg", 0, 0, tiled=True)
    width = maps.shape[-1]
    prefix = jnp.broadcast_to(jnp.eye(width, dtype=jnp.float32), maps.shape)
    for step in range(segments - 1):
        grown = mm("kab,kbc->kac", prefix, every[step], EXACT)
        prefix = jnp.where(step < segment, grown, prefix)
    right_side = mm("wkbc,kcd->wkbd", left_env, prefix)
    return mm("kba,wkbd->wkad", prefix, right_side)


def exchange(vector, right):
    products = mm("kab,wkbc->wkac", vector, right)
    from_left = shifted(products[0::3, 1], "sec", 1)
    from_right = shifted(products[2::3, 0], "sec", -1)
    return products, from_left, from_right


def combine(parts, ordered):
    products, from_left, from_right = parts
    lower = jnp.stack([from_left, products[0::3, 0]], axis=1)
    upper = jnp.stack([products[2::3, 1], from_right], axis=1)
    terms = jnp.concatenate([lower, products[1::3], upper], axis=0)
    return mm("wkab,wkbc->kac", ordered, terms)


def split_image(parts, ordered):
    products, from_left, from_right = parts
    group = ordered.shape[0] // 3
    blank = jnp.zeros_like(from_left)
    inner = combine((products, blank, blank), ordered)
    lower = inner[0] + mm("wab,wbc->ac", ordered[:group, 0], from_left)
    upper = inner[1] + mm("wab,wbc->ac", ordered[2 * group :, 1], from_right)
    return jnp.stack([lower, upper], axis=0)


def apply_terms(vector, right, ordered, split=False):
    if not split:
        return combine(exchange(vector, right), ordered)
    return split_image(exchange(vector, right), ordered)


def square_sums(normal, lifted):
    stacked = jnp.stack([normal, lifted, lifted * SHRINK], axis=0)
    return jnp.sum(stacked * stacked, axis=(1, 2, 3))


def scales(sums, cells):
    first = lax.rsqrt(sums[0] / cells + EPS)
    step = first / LIFT
    plain = step * step * sums[1]
    shrunk = jnp.square(step / SHRINK) * sums[2]
    second = lax.rsqrt(jnp.where(jnp.isfinite(sums[1]), plain, shrunk) / cells + EPS)
    return first, second


def per_device(theta_in, left_env, site_maps, right_env, mpo_mask, ranks):
    vector = theta_in[0]
    maps = site_maps[0]
    right = right_env[0]
    blocks = vector.shape[0]
    width = vector.shape[1]
    cells = lax.axis_size("sec") * blocks * width * width
    env = left_environment(left_env, maps)
    weighted = env * mpo_mask.astype(jnp.float32)[:, :, None, None]
    ordered = jnp.concatenate([weighted[0::3], weighted[1::3], weighted[2::3]], axis=0)
    current = apply_terms(vector, right, ordered)
    rows = lax.broadcasted_iota(jnp.int32, (blocks, width), 1) < ranks[0][:, None]
    for pair in range(ITERS // 2):
        lifted = apply_terms(current * LIFT, right, ordered, split=True)
        more = 2 * pair + 2 < ITERS
        if more:
            parts = exchange(lifted * LIFT, right)
        else:
            trimmed = lifted * rows.astype(jnp.float32)[:, :, None]
            peak = jnp.maximum(jnp.max(jnp.abs(trimmed)), jnp.finfo(jnp.float32).tiny)
            unit = trimmed * (1.0 / peak)
            gram, peak = lax.optimization_barrier((mm("kab,kcb->kac", unit, unit), peak))
        first, second = scales(gathered_sums(square_sums(current, lifted), "sec"), cells)
        if more:
            current = split_image(parts, ordered * (first / LIFT)) * (second / LIFT)
        else:
            factor = (first / LIFT) * second
            current = lifted * factor
            density = gram * (jnp.square(factor * peak) / width)
    return (current[None], density[None])


def solution(mesh):
    return jax.shard_map(
        per_device,
        mesh=mesh,
        in_specs=(
            P("seg", "sec", None, None),
            P(None, "sec", None, None),
            P("seg", "sec", None, None),
            P("seg", None, "sec", None, None),
            P(None, "sec"),
            P("seg", "sec"),
        ),
        out_specs=(P("seg", "sec", None, None), P("seg", "sec", None, None)),
        check_vma=False,
    )
```
